1024 devices in a mesh: ctx: 32 (over z_lo, x, core), exp: 8 (over y), dp: 4 (over z_hi).
Axes of the slice: x: 4, y: 8, z: 16 (z_hi: 4, z_lo: 4; z = z_hi * 4 + z_lo), core: 2. Of those that a mesh axis runs over, the one named last changes fastest.
Arguments:
- queries: bfloat16 [4, 8192, 6144], P('dp', 'ctx', 'exp'), may hold values from -4 to 4
- key_rows: bfloat16 [4, 8192, 1024], P('dp', 'ctx', 'exp'), may hold values from -4 to 4
- value_rows: bfloat16 [4, 8192, 1024], P('dp', 'ctx', 'exp'), may hold values from -6 to 6
- out_grad: bfloat16 [4, 8192, 6144], P('dp', 'ctx', 'exp'), may hold values from -6 to 6
- log_norm: float32 [4, 48, 8192], P('dp', 'exp', 'ctx'), may hold values from 1 to 3
- row_delta: float32 [4, 48, 8192], P('dp', 'exp', 'ctx'), may hold values from -16 to 16
- tok_grad: bfloat16 [4, 8192, 6144], P('dp', ('ctx', 'exp')), may hold values from -6 to 6
- router_prob: float32 [4, 8192, 2], P('dp', ('ctx', 'exp')), may hold values from 0.2 to 1
- expert_ids: int32 [4, 8192, 2], P('dp', ('ctx', 'exp')), may hold values from 0 to 7, all different within a row; in each aligned block of 32 rows (0 to 31, 32 to 63, ..., all dimensions but the last counted through in order) at most 16 rows name the same one
- saved_pre: bfloat16 [8, 32, 4, 128, 256], P('exp', 'ctx', 'dp'), may hold values from -4 to 4
- w_down: bfloat16 [8, 128, 6144], P('exp'), may hold values from -0.078125 to 0.078125
Outputs:
- query_grad: bfloat16 [4, 8192, 6144], P('dp', 'ctx', 'exp')
- key_grad: bfloat16 [4, 8192, 1024], P('dp', 'ctx', 'exp')
- value_grad: bfloat16 [4, 8192, 1024], P('dp', 'ctx', 'exp')
- pre_grad: bfloat16 [8, 32, 4, 128, 256], P('exp', 'ctx', 'dp')
- weight_grad: float32 [8, 6144, 128], P('exp', ('ctx', 'dp'))
The draws below stay inside these ranges and needn't reach their ends.
Inputs may be any that keep to these rules, and one draw needn't show every extreme that they name: `expert_ids`: the two experts of a token differ; among the 32 tokens of one device each expert is named by at most 16 tokens, a bound that some block reaches.
All inputs are finite; a program needn't handle non-finite values.
Results may differ from the reference program's by a relative error of at most 0.0068.
Values may be sent and summed in bfloat16 or wider, within the bound.
No kernel may reach another device: no remote copies, remote signals or barrier semaphores. Data moves between devices by JAX's collectives and lax.ppermute only.
A program may use at most 32 MiB of HBM per device.

```python
import math
import jax
import jax.numpy as jnp
import numpy as np
from jax import lax

D = 6144
HEADS = 48
KV_HEADS = 8
HEAD_DIM = 128
FF_WIN = 128
TOK = 256
SEQ = 8192
EXPERTS = 8
MOE_TOK = 32
CAP = 16
SLOTS = 128
N_CTX = 32
N_EXP = 8
N_DP = 4


def level_of(rng, dims, split, low, largest):
    def one(dim, parts):
        heights = jax.random.uniform(jax.random.fold_in(jax.random.fold_in(rng, 6), dim), (parts,), jnp.float32, low / len(split), largest / len(split))
        return jnp.repeat(jnp.exp(heights), dims[dim] // parts).reshape((-1,) + (1,) * (len(dims) - dim - 1))

    gain = one(*split[0])
    for cut in split[1:]:
        gain = gain * one(*cut)
    return gain


def routed_block(stream_key, own, number, rows, amount, top, reach, skew):
    sequence = jax.random.permutation(stream_key, amount)
    heavy_load, ordinary = shares(amount, rows * top, reach, skew, True), shares(amount, rows * top, reach, skew, False)
    places = jnp.arange(amount)

    def named(tallies, turn):
        used = int((tallies > 0).sum())
        fixed = max(1, used // 4)
        shifted = fixed + (places - fixed + turn * (used - fixed)) % max(1, amount - fixed)
        return jnp.zeros((amount,), jnp.int32).at[sequence[jnp.where(places < fixed, places, shifted)]].set(jnp.asarray(tallies, jnp.int32))

    tallies = jnp.where(number % 4 == 0, named(heavy_load, number // 4), named(ordinary, number - number // 4 - 1))
    mixed = jax.random.permutation(jax.random.fold_in(own, 3), amount)
    giver, receiver = mixed[0:amount // 2 * 2:2], mixed[1:amount // 2 * 2:2]
    margin = jnp.minimum(tallies[giver] - 1, reach - tallies[receiver]) // 2
    margin = jnp.where((giver == sequence[0]) | (receiver == sequence[0]) | (tallies[receiver] == 0), 0, jnp.maximum(margin, 0))
    shifted = jax.random.randint(jax.random.fold_in(own, 4), (amount // 2,), 0, 1 << 20) % (margin + 1)
    tallies = tallies.at[giver].add(-shifted).at[receiver].add(shifted)
    members = jnp.searchsorted(jnp.cumsum(tallies), jnp.arange(rows * top), side="right").astype(jnp.int32)
    table = members.reshape(top, rows).T
    table = table[jax.random.permutation(jax.random.fold_in(own, 1), rows)]
    turn = jax.random.randint(jax.random.fold_in(own, 2), (rows, 1), 0, top)
    return jnp.take_along_axis(table, (jnp.arange(top)[None, :] + turn) % top, axis=1)


def shares(count, total, limit, skew, full):
    loads = [(1 << 20) // math.isqrt(standing ** skew) + 1 for standing in range(1, count + 1)]
    largest = limit if full else min(limit, max(-(-total // count), total * loads[0] // sum(loads)))
    least = 1 if total - largest >= count - 1 else 0
    holding, spare = [largest] + [least] * (count - 1), total - largest - least * (count - 1)
    while spare > 0:
        candidates = [i for i in range(1, count) if holding[i] < largest] or [i for i in range(1, count) if holding[i] < limit]
        whole, budget = sum([loads[i] for i in candidates]), spare
        for i in candidates:
            more = min(limit - holding[i], max(1, budget * loads[i] // whole), spare)
            holding[i] = holding[i] + more
            spare = spare - more
    return np.array(holding)


def scatter_about(stream_key, extent, width, most, pieces=(), kind=jnp.bfloat16):
    result = jax.random.normal(stream_key, extent, jnp.float32) * width
    if len(pieces) > 0:
        result = level_of(stream_key, extent, pieces, -0.22, 0.18) * result
    return jnp.clip(result, min=-most, max=most).astype(kind)


def setup_inputs(seed: int = 0) -> dict:
    key_of = jax.random.split(jax.random.key(seed), 12)
    queries = scatter_about(key_of[0], (N_DP, SEQ, HEADS * HEAD_DIM), 1.0, 4.0, ((0, 4), (1, 32), (2, 8)))
    key_rows = scatter_about(key_of[1], (N_DP, SEQ, KV_HEADS * HEAD_DIM), 1.0, 4.0, ((0, 4), (1, 32), (2, 8)))
    value_rows = scatter_about(key_of[2], (N_DP, SEQ, KV_HEADS * HEAD_DIM), 1.0, 6.0, ((0, 4), (1, 32), (2, 8)))
    out_grad = scatter_about(key_of[3], (N_DP, SEQ, HEADS * HEAD_DIM), 1.0, 6.0, ((0, 4), (1, 32), (2, 8)))
    log_norm = jnp.clip(1.0 + 2.0 * jax.random.uniform(key_of[4], (N_DP, HEADS, SEQ), jnp.float32) ** level_of(key_of[4], (N_DP, HEADS, SEQ), ((0, 4), (1, 8), (2, 32)), -0.2, 0.2), 1.0, 3.0)
    row_delta = scatter_about(key_of[5], (N_DP, HEADS, SEQ), 4.0, 16.0, ((0, 4), (1, 8), (2, 32)), jnp.float32)
    tok_grad = scatter_about(key_of[6], (N_DP, SEQ, D), 1.0, 6.0, ((0, 4), (1, 256)))
    router_prob = jnp.clip(0.2 + 0.8 * jax.random.uniform(key_of[7], (N_DP, SEQ, 2), jnp.float32) ** level_of(key_of[7], (N_DP, SEQ, 2), ((0, 4), (1, 256)), -0.2, 0.2), 0.2, 1.0)
    expert_ids_keys = jax.random.split(jax.random.fold_in(key_of[8], 1), N_DP * SEQ // MOE_TOK)
    expert_ids_turns = jax.random.permutation(jax.random.fold_in(key_of[8], 3), N_DP * SEQ // MOE_TOK)
    expert_ids = jax.vmap(lambda own, number: routed_block(jax.random.fold_in(key_of[8], 2), own, number, MOE_TOK, EXPERTS, 2, CAP, 2))(expert_ids_keys, expert_ids_turns).reshape((N_DP, SEQ, 2))
    saved_pre = scatter_about(key_of[9], (EXPERTS, N_CTX, N_DP, SLOTS, 2 * FF_WIN), 1.0, 4.0, ((0, 8), (1, 32), (2, 4)))
    w_down = scatter_about(key_of[10], (EXPERTS, FF_WIN, D), D ** -0.5, 0.078125, ((0, 8),))
    return {"queries": queries, "key_rows": key_rows, "value_rows": value_rows, "out_grad": out_grad, "log_norm": log_norm, "row_delta": row_delta, "tok_grad": tok_grad, "router_prob": router_prob, "expert_ids": expert_ids, "saved_pre": saved_pre, "w_down": w_down}


def pair_grads(query_blk, grad_blk, norm_blk, delta_blk, key_blk, value_blk):
    length = query_blk.shape[0]
    group_size = HEADS // KV_HEADS
    factor = HEAD_DIM ** -0.5
    query_full = query_blk.astype(jnp.float32).reshape(length, KV_HEADS, group_size, HEAD_DIM)
    grad_full = grad_blk.astype(jnp.float32).reshape(length, KV_HEADS, group_size, HEAD_DIM)
    key_full = key_blk.astype(jnp.float32).reshape(length, KV_HEADS, HEAD_DIM)
    value_full = value_blk.astype(jnp.float32).reshape(length, KV_HEADS, HEAD_DIM)
    norm_rows = norm_blk.reshape(KV_HEADS, group_size, length)[..., None]
    delta_rows = delta_blk.reshape(KV_HEADS, group_size, length)[..., None]
    scores = jnp.einsum('tkgd,ukd->kgtu', query_full, key_full) * factor
    weights = jnp.exp(scores - norm_rows)
    weights_low = lax.optimization_barrier(weights.astype(jnp.bfloat16)).astype(jnp.float32)
    prob_grad = jnp.einsum('tkgd,ukd->kgtu', grad_full, value_full)
    score_grad = (weights * (prob_grad - delta_rows)).astype(jnp.bfloat16)
    score_grad = lax.optimization_barrier(score_grad).astype(jnp.float32)
    query_portion = jnp.einsum('kgtu,ukd->tkgd', score_grad, key_full) * factor
    key_part = jnp.einsum('kgtu,tkgd->ukd', score_grad, query_full) * factor
    value_part = jnp.einsum('kgtu,tkgd->ukd', weights_low, grad_full)
    return (query_portion.reshape(length, HEADS * HEAD_DIM),
            key_part.reshape(length, KV_HEADS * HEAD_DIM),
            value_part.reshape(length, KV_HEADS * HEAD_DIM))


def attention_grads(queries, key_rows, value_rows, out_grad, log_norm, row_delta):
    def sequence_wise(items):
        query_seq, key_seq, value_seq, grad_seq, norm_seq, delta_seq = items

        def per_block(block):
            first = block * TOK
            near = jnp.maximum(block - 1, 0) * TOK
            far = jnp.maximum(block - 2, 0) * TOK
            query_blk = lax.dynamic_slice_in_dim(query_seq, first, TOK, 0)
            grad_blk = lax.dynamic_slice_in_dim(grad_seq, first, TOK, 0)
            norm_blk = lax.dynamic_slice_in_dim(norm_seq, first, TOK, 1)
            delta_blk = lax.dynamic_slice_in_dim(delta_seq, first, TOK, 1)
            near_mask = (block >= 1).astype(jnp.float32)
            far_mask = (block >= 2).astype(jnp.float32)
            query_near, key_near, value_near = pair_grads(
                query_blk, grad_blk, norm_blk, delta_blk,
                lax.dynamic_slice_in_dim(key_seq, near, TOK, 0),
                lax.dynamic_slice_in_dim(value_seq, near, TOK, 0))
            query_far, key_far, value_far = pair_grads(
                query_blk, grad_blk, norm_blk, delta_blk,
                lax.dynamic_slice_in_dim(key_seq, far, TOK, 0),
                lax.dynamic_slice_in_dim(value_seq, far, TOK, 0))
            query_total = (query_near * near_mask + query_far * far_mask).astype(jnp.bfloat16)
            return (query_total, (key_near * near_mask).astype(jnp.bfloat16),
                    (value_near * near_mask).astype(jnp.bfloat16), key_far * far_mask, value_far * far_mask)

        blocks = jnp.arange(N_CTX, dtype=jnp.int32)
        query_out, key_near, value_near, key_far, value_far = lax.map(per_block, blocks)
        key_prev = jnp.roll(key_near, 1, axis=0)
        value_prev = jnp.roll(value_near, 1, axis=0)
        key_out = (key_prev.astype(jnp.float32) + key_far).astype(jnp.bfloat16)
        value_out = (value_prev.astype(jnp.float32) + value_far).astype(jnp.bfloat16)
        return (query_out.reshape(SEQ, HEADS * HEAD_DIM),
                key_out.reshape(SEQ, KV_HEADS * HEAD_DIM),
                value_out.reshape(SEQ, KV_HEADS * HEAD_DIM))

    return lax.map(sequence_wise, (queries, key_rows, value_rows, out_grad, log_norm, row_delta))


def route_rows(expert_selection, router_sel, grad_sel):
    pair_count = expert_selection.shape[0] * 2
    routed = (router_sel[:, :, None] * grad_sel.astype(jnp.float32)[:, None, :]).astype(jnp.bfloat16)
    routed = routed.reshape(pair_count, D)
    flat_ids = expert_selection.reshape(pair_count)
    matches = (flat_ids[:, None] == jnp.arange(EXPERTS, dtype=jnp.int32)[None, :]).astype(jnp.int32)
    earlier = jnp.cumsum(matches, axis=0) - matches
    place = jnp.sum(earlier * matches, axis=1)
    slot_index = flat_ids * CAP + place
    table = (jnp.arange(EXPERTS * CAP, dtype=jnp.int32)[:, None] == slot_index[None, :]).astype(jnp.bfloat16)
    return jnp.dot(table, routed, preferred_element_type=jnp.float32).astype(jnp.bfloat16)


def expert_grads(tok_grad, router_prob, expert_ids, saved_pre, w_down):
    zero = jnp.zeros((), jnp.int32)
    down_weight_complete = w_down.astype(jnp.float32)

    def per_group(total, group):
        block = group // N_DP
        seq_index = group % N_DP
        first = block * TOK
        grad_blk = lax.dynamic_slice(tok_grad, (seq_index, first, zero), (1, TOK, D)).reshape(N_EXP, MOE_TOK, D)
        prob_blk = lax.dynamic_slice(router_prob, (seq_index, first, zero), (1, TOK, 2)).reshape(N_EXP, MOE_TOK, 2)
        ids_blk = lax.dynamic_slice(expert_ids, (seq_index, first, zero), (1, TOK, 2)).reshape(N_EXP, MOE_TOK, 2)
        sends = jax.vmap(route_rows)(ids_blk, prob_blk, grad_blk)
        incoming_block = sends.reshape(N_EXP, EXPERTS, CAP, D).transpose(1, 0, 2, 3).reshape(EXPERTS, SLOTS, D)
        incoming_block = incoming_block.astype(jnp.float32)
        saved = lax.dynamic_slice(saved_pre, (zero, block, seq_index, zero, zero),
                                  (EXPERTS, 1, 1, SLOTS, 2 * FF_WIN)).reshape(EXPERTS, SLOTS, 2 * FF_WIN)
        saved = saved.astype(jnp.float32)
        gate = saved[..., :FF_WIN]
        upward = saved[..., FF_WIN:]
        sigma = jax.nn.sigmoid(gate)
        active = gate * sigma
        hidden_state = lax.optimization_barrier((active * upward).astype(jnp.bfloat16)).astype(jnp.float32)
        hidden_gradient = jnp.einsum('ecu,emu->ecm', incoming_block, down_weight_complete)
        gate_grad = hidden_gradient * upward * sigma * (1.0 + gate * (1.0 - sigma))
        up_grad = hidden_gradient * active
        pre_out = jnp.concatenate([gate_grad, up_grad], axis=-1).astype(jnp.bfloat16)
        gradient_addend = jnp.einsum('hjv,hjm->hvm', incoming_block, hidden_state)
        return total + gradient_addend, pre_out

    start = jnp.zeros((EXPERTS, D, FF_WIN), jnp.float32)
    groups = jnp.arange(N_CTX * N_DP, dtype=jnp.int32)
    total, pre_all = lax.scan(per_group, start, groups)
    weight_grad = total * (1.0 / (N_CTX * N_DP))
    pre_grad = pre_all.reshape(N_CTX, N_DP, EXPERTS, SLOTS, 2 * FF_WIN).transpose(2, 0, 1, 3, 4)
    return pre_grad, weight_grad


def reference(queries, key_rows, value_rows, out_grad, log_norm, row_delta, tok_grad, router_prob, expert_ids, saved_pre, w_down):
    query_grad, key_grad, value_grad = attention_grads(queries, key_rows, value_rows, out_grad, log_norm, row_delta)
    pre_grad, weight_grad = expert_grads(tok_grad, router_prob, expert_ids, saved_pre, w_down)
    return (query_grad, key_grad, value_grad, pre_grad, weight_grad)
```

```python
import jax
import jax.numpy as jnp
from jax import lax
from jax.sharding import Mesh, PartitionSpec as P

HEADS = 48
KV_HEADS = 8
HEAD_DIM = 128
CTX = ("zl", "xx", "core")
ROW_AXES = ("zl", "xx", "core", "dp")


def passed_along(value, axis, by):
    size = lax.axis_size(axis)
    pairs = [(i, i + by) for i in range(size) if 0 <= i + by < size]
    return lax.ppermute(value, axis, pairs)


def from_behind(block, axis, distance):
    devices = range(lax.axis_size(axis))
    route = [((i - distance) % len(devices), i) for i in devices]
    return lax.ppermute(block, axis, route)


def pair_grads(query_rows, grad_rows, norm_rows, delta_rows, both_block):
    head_sets = query_rows.shape[0]
    length = both_block.shape[1]
    factor = HEAD_DIM ** (-0.5)
    key_part = both_block[0].reshape(length, head_sets, HEAD_DIM).transpose(1, 0, 2)
    value_part = both_block[1].reshape(length, head_sets, HEAD_DIM).transpose(1, 0, 2)
    scores = (
        jnp.einsum("kqd,kud->kqu", query_rows, key_part, preferred_element_type=jnp.float32)
        * factor
    )
    weights = jnp.exp(scores - norm_rows[:, :, None])
    weights_low = weights.astype(jnp.bfloat16)
    prob_grad = jnp.einsum(
        "kqd,kud->kqu", grad_rows, value_part, preferred_element_type=jnp.float32
    )
    score_grad = (weights * (prob_grad - delta_rows[:, :, None])).astype(jnp.bfloat16)
    query_out = (
        jnp.einsum("kqu,kud->kqd", score_grad, key_part, preferred_element_type=jnp.float32)
        * factor
    )
    key_out = (
        jnp.einsum("kqu,kqd->kud", score_grad, query_rows, preferred_element_type=jnp.float32)
        * factor
    )
    value_out = jnp.einsum(
        "kqu,kqd->kud", weights_low, grad_rows, preferred_element_type=jnp.float32
    )
    return (query_out, key_out, value_out)


def staged_reduce_scatter(partial):
    rows, width = partial.shape
    sizes = [lax.axis_size(name) for name in ROW_AXES]
    block = rows // (sizes[0] * sizes[1] * sizes[2] * sizes[3])
    pieces = partial.reshape(*sizes, block, width).transpose(2, 1, 0, 3, 4, 5)
    for name in ("core", "xx", "zl", "dp"):
        pieces = lax.all_to_all(pieces, name, 0, 0, tiled=True).sum(0)
    return pieces.reshape(block, width)


def body(
    queries,
    key_rows,
    value_rows,
    out_grad,
    log_norm,
    row_delta,
    tok_grad,
    router_prob,
    expert_ids,
    saved_pre,
    w_down,
):
    length = queries.shape[1]
    head_sets = key_rows.shape[2] // HEAD_DIM
    group_size = HEADS // KV_HEADS
    position = lax.axis_index(CTX)

    def by_head(array):
        shaped = array[0].reshape(length, head_sets, group_size, HEAD_DIM).transpose(1, 2, 0, 3)
        return shaped.reshape(head_sets, group_size * length, HEAD_DIM)

    query_rows = by_head(queries)
    grad_rows = by_head(out_grad)
    norm_rows = log_norm[0].reshape(head_sets, group_size * length)
    delta_rows = row_delta[0].reshape(head_sets, group_size * length)
    both_local = jnp.stack([key_rows[0], value_rows[0]])
    carried_blocks = []
    current = both_local
    for repeat in range(2):
        current = passed_along(current, CTX, 1)
        carried_blocks.append(current)
    nearer = carried_blocks[0]
    farther = carried_blocks[1]
    near_mask = (position >= 1).astype(jnp.float32)
    far_mask = (position >= 2).astype(jnp.float32)
    query_near, key_near, value_near = pair_grads(
        query_rows, grad_rows, norm_rows, delta_rows, nearer
    )
    outgoing = (jnp.stack([key_near, value_near]) * near_mask).astype(jnp.bfloat16)
    arrived = from_behind(outgoing, CTX, 1)
    query_far, key_far, value_far = pair_grads(
        query_rows, grad_rows, norm_rows, delta_rows, farther
    )
    query_total = query_near * near_mask + query_far * far_mask
    query_grad = query_total.reshape(head_sets, group_size, length, HEAD_DIM).transpose(2, 0, 1, 3)
    query_grad = query_grad.reshape(1, length, head_sets * group_size * HEAD_DIM).astype(
        jnp.bfloat16
    )
    both_total = (arrived.astype(jnp.float32) + jnp.stack([key_far, value_far]) * far_mask).astype(
        jnp.bfloat16
    )
    key_grad = both_total[0].transpose(1, 0, 2).reshape(1, length, head_sets * HEAD_DIM)
    value_grad = both_total[1].transpose(1, 0, 2).reshape(1, length, head_sets * HEAD_DIM)
    expert_count = lax.axis_size("exp")
    capacity = saved_pre.shape[3] // expert_count
    model_width = tok_grad.shape[2]
    pair_count = tok_grad.shape[1] * 2
    routed = (router_prob[0][:, :, None] * tok_grad[0].astype(jnp.float32)[:, None, :]).astype(
        jnp.bfloat16
    )
    routed = routed.reshape(pair_count, model_width)
    flat_ids = expert_ids[0].reshape(pair_count)
    matches = (flat_ids[:, None] == jnp.arange(expert_count, dtype=jnp.int32)[None, :]).astype(
        jnp.int32
    )
    earlier = jnp.cumsum(matches, axis=0) - matches
    place = jnp.sum(earlier * matches, axis=1)
    slot_index = flat_ids * capacity + place
    table = (
        jnp.arange(expert_count * capacity, dtype=jnp.int32)[:, None] == slot_index[None, :]
    ).astype(jnp.bfloat16)
    outbound = jnp.dot(table, routed, preferred_element_type=jnp.float32).astype(jnp.bfloat16)
    incoming_block = lax.all_to_all(outbound, "exp", split_axis=0, concat_axis=0, tiled=True)
    saved = saved_pre[0, 0, 0].astype(jnp.float32)
    hidden_units = saved.shape[1] // 2
    gate = saved[:, :hidden_units]
    upward = saved[:, hidden_units:]
    sigma = jax.nn.sigmoid(gate)
    active = gate * sigma
    hidden_state = (active * upward).astype(jnp.bfloat16)
    hidden_gradient = jnp.einsum(
        "rd,fd->rf", incoming_block, w_down[0], preferred_element_type=jnp.float32
    )
    gate_grad = hidden_gradient * upward * sigma * (1.0 + gate * (1.0 - sigma))
    up_grad = hidden_gradient * active
    pre_grad = jnp.concatenate([gate_grad, up_grad], axis=-1).astype(jnp.bfloat16)[None, None, None]
    averaging = 1.0 / lax.axis_size(ROW_AXES)
    partial = jnp.einsum("rc,rf->cf", incoming_block, hidden_state, preferred_element_type=jnp.float32)
    summed = staged_reduce_scatter(partial)
    weight_grad = (summed * averaging)[None]
    return (query_grad, key_grad, value_grad, pre_grad, weight_grad)


def solution(mesh):
    placed = (
        P("dp", CTX, "exp"),
        P("dp", CTX, "exp"),
        P("dp", CTX, "exp"),
        P("dp", CTX, "exp"),
        P("dp", "exp", CTX),
        P("dp", "exp", CTX),
        P("dp", CTX + ("exp",), None),
        P("dp", CTX + ("exp",), None),
        P("dp", CTX + ("exp",), None),
        P("exp", CTX, "dp", None, None),
        P("exp", None, None),
    )
    ctx_size, exp_size, dp_size = mesh.devices.shape
    split = Mesh(
        mesh.devices.reshape(ctx_size // 8, 4, 2, exp_size, dp_size), ("zl", "xx", "core", "exp", "dp")
    )
    return jax.shard_map(
        body,
        mesh=split,
        in_specs=placed,
        out_specs=(
            P("dp", CTX, "exp"),
            P("dp", CTX, "exp"),
            P("dp", CTX, "exp"),
            P("exp", CTX, "dp", None, None),
            P("exp", ROW_AXES, None),
        ),
        check_vma=False,
    )
```

```python
import jax
import jax.numpy as jnp
from jax import lax
from jax.sharding import Mesh, PartitionSpec as P

HEADS = 48
KV_HEADS = 8
HEAD_DIM = 128
CTX = ("zl", "xx", "core")
ROW_AXES = ("zl", "xx", "core", "dp")


def passed_along(value, axis, by):
    size = lax.axis_size(axis)
    pairs = [(i, i + by) for i in range(size) if 0 <= i + by < size]
    return lax.ppermute(value, axis, pairs)


def from_behind(block, axis, distance):
    devices = range(lax.axis_size(axis))
    route = [((i - distance) % len(devices), i) for i in devices]
    return lax.ppermute(block, axis, route)


def pair_grads(query_rows, grad_rows, norm_rows, delta_rows, both_block):
    head_sets = query_rows.shape[0]
    length = both_block.shape[1]
    factor = HEAD_DIM ** (-0.5)
    key_part = both_block[0].reshape(length, head_sets, HEAD_DIM).transpose(1, 0, 2)
    value_part = both_block[1].reshape(length, head_sets, HEAD_DIM).transpose(1, 0, 2)
    scores = (
        jnp.einsum("kqd,kud->kqu", query_rows, key_part, preferred_element_type=jnp.float32)
        * factor
    )
    weights = jnp.exp(scores - norm_rows[:, :, None])
    weights_low = weights.astype(jnp.bfloat16)
    prob_grad = jnp.einsum(
        "kqd,kud->kqu", grad_rows, value_part, preferred_element_type=jnp.float32
    )
    score_grad = (weights * (prob_grad - delta_rows[:, :, None])).astype(jnp.bfloat16)
    query_out = (
        jnp.einsum("kqu,kud->kqd", score_grad, key_part, preferred_element_type=jnp.float32)
        * factor
    )
    key_out = (
        jnp.einsum("kqu,kqd->kud", score_grad, query_rows, preferred_element_type=jnp.float32)
        * factor
    )
    value_out = jnp.einsum(
        "kqu,kqd->kud", weights_low, grad_rows, preferred_element_type=jnp.float32
    )
    return (query_out, key_out, value_out)


def weight_partial_sums(incoming_block, hidden_state):
    slots, width = incoming_block.shape
    zl, xx, core, dp = (lax.axis_size(name) for name in ROW_AXES)
    block = width // (zl * xx * core * dp)
    columns = incoming_block.reshape(slots, zl, xx, core, dp, block)
    here = lax.axis_index("core")
    swap = [(i, (i + 1) % core) for i in range(core)]
    mine = lax.dynamic_index_in_dim(columns, here, 3, keepdims=False)
    other = lax.dynamic_index_in_dim(columns, 1 - here, 3, keepdims=False)
    rows_in = jnp.concatenate([mine, lax.ppermute(other, "core", swap)], axis=0)
    hidden_in = jnp.concatenate([hidden_state, lax.ppermute(hidden_state, "core", swap)], axis=0)
    pieces = jnp.einsum(
        "rzxdq,rf->xzdqf", rows_in, hidden_in, preferred_element_type=jnp.float32
    )
    pieces = lax.all_to_all(pieces, "xx", 0, 0, tiled=True).sum(0)
    pieces = pieces.reshape(zl * dp, block, hidden_state.shape[1])
    pieces = lax.all_to_all(pieces, ("zl", "dp"), 0, 0, tiled=True).sum(0)
    return pieces


def body(
    queries,
    key_rows,
    value_rows,
    out_grad,
    log_norm,
    row_delta,
    tok_grad,
    router_prob,
    expert_ids,
    saved_pre,
    w_down,
):
    length = queries.shape[1]
    head_sets = key_rows.shape[2] // HEAD_DIM
    group_size = HEADS // KV_HEADS
    position = lax.axis_index(CTX)

    def by_head(array):
        shaped = array[0].reshape(length, head_sets, group_size, HEAD_DIM).transpose(1, 2, 0, 3)
        return shaped.reshape(head_sets, group_size * length, HEAD_DIM)

    query_rows = by_head(queries)
    grad_rows = by_head(out_grad)
    norm_rows = log_norm[0].reshape(head_sets, group_size * length)
    delta_rows = row_delta[0].reshape(head_sets, group_size * length)
    both_local = jnp.stack([key_rows[0], value_rows[0]])
    carried_blocks = []
    current = both_local
    for repeat in range(2):
        current = passed_along(current, CTX, 1)
        carried_blocks.append(current)
    nearer = carried_blocks[0]
    farther = carried_blocks[1]
    near_mask = (position >= 1).astype(jnp.float32)
    far_mask = (position >= 2).astype(jnp.float32)
    query_near, key_near, value_near = pair_grads(
        query_rows, grad_rows, norm_rows, delta_rows, nearer
    )
    outgoing = (jnp.stack([key_near, value_near]) * near_mask).astype(jnp.bfloat16)
    arrived = from_behind(outgoing, CTX, 1)
    query_far, key_far, value_far = pair_grads(
        query_rows, grad_rows, norm_rows, delta_rows, farther
    )
    query_total = query_near * near_mask + query_far * far_mask
    query_grad = query_total.reshape(head_sets, group_size, length, HEAD_DIM).transpose(2, 0, 1, 3)
    query_grad = query_grad.reshape(1, length, head_sets * group_size * HEAD_DIM).astype(
        jnp.bfloat16
    )
    both_total = (arrived.astype(jnp.float32) + jnp.stack([key_far, value_far]) * far_mask).astype(
        jnp.bfloat16
    )
    key_grad = both_total[0].transpose(1, 0, 2).reshape(1, length, head_sets * HEAD_DIM)
    value_grad = both_total[1].transpose(1, 0, 2).reshape(1, length, head_sets * HEAD_DIM)
    expert_count = lax.axis_size("exp")
    capacity = saved_pre.shape[3] // expert_count
    model_width = tok_grad.shape[2]
    pair_count = tok_grad.shape[1] * 2
    routed = (router_prob[0][:, :, None] * tok_grad[0].astype(jnp.float32)[:, None, :]).astype(
        jnp.bfloat16
    )
    routed = routed.reshape(pair_count, model_width)
    flat_ids = expert_ids[0].reshape(pair_count)
    matches = (flat_ids[:, None] == jnp.arange(expert_count, dtype=jnp.int32)[None, :]).astype(
        jnp.int32
    )
    earlier = jnp.cumsum(matches, axis=0) - matches
    place = jnp.sum(earlier * matches, axis=1)
    slot_index = flat_ids * capacity + place
    table = (
        jnp.arange(expert_count * capacity, dtype=jnp.int32)[:, None] == slot_index[None, :]
    ).astype(jnp.bfloat16)
    outbound = jnp.dot(table, routed, preferred_element_type=jnp.float32).astype(jnp.bfloat16)
    incoming_block = lax.all_to_all(outbound, "exp", split_axis=0, concat_axis=0, tiled=True)
    saved = saved_pre[0, 0, 0].astype(jnp.float32)
    hidden_units = saved.shape[1] // 2
    gate = saved[:, :hidden_units]
    upward = saved[:, hidden_units:]
    sigma = jax.nn.sigmoid(gate)
    active = gate * sigma
    hidden_state = (active * upward).astype(jnp.bfloat16)
    hidden_gradient = jnp.einsum(
        "rd,fd->rf", incoming_block, w_down[0], preferred_element_type=jnp.float32
    )
    gate_grad = hidden_gradient * upward * sigma * (1.0 + gate * (1.0 - sigma))
    up_grad = hidden_gradient * active
    pre_grad = jnp.concatenate([gate_grad, up_grad], axis=-1).astype(jnp.bfloat16)[None, None, None]
    averaging = 1.0 / lax.axis_size(ROW_AXES)
    summed = weight_partial_sums(incoming_block, hidden_state)
    weight_grad = (summed * averaging)[None]
    return (query_grad, key_grad, value_grad, pre_grad, weight_grad)


def solution(mesh):
    placed = (
        P("dp", CTX, "exp"),
        P("dp", CTX, "exp"),
        P("dp", CTX, "exp"),
        P("dp", CTX, "exp"),
        P("dp", "exp", CTX),
        P("dp", "exp", CTX),
        P("dp", CTX + ("exp",), None),
        P("dp", CTX + ("exp",), None),
        P("dp", CTX + ("exp",), None),
        P("exp", CTX, "dp", None, None),
        P("exp", None, None),
    )
    ctx_size, exp_size, dp_size = mesh.devices.shape
    split = Mesh(
        mesh.devices.reshape(ctx_size // 8, 4, 2, exp_size, dp_size), ("zl", "xx", "core", "exp", "dp")
    )
    return jax.shard_map(
        body,
        mesh=split,
        in_specs=placed,
        out_specs=(
            P("dp", CTX, "exp"),
            P("dp", CTX, "exp"),
            P("dp", CTX, "exp"),
            P("exp", CTX, "dp", None, None),
            P("exp", ROW_AXES, None),
        ),
        check_vma=False,
    )
```

```python
import jax
import jax.numpy as jnp
from jax import lax
from jax.sharding import Mesh, PartitionSpec as P

HEADS = 48
KV_HEADS = 8
HEAD_DIM = 128
CTX = ("zl", "xx", "core")
ROW_AXES = ("zl", "xx", "core", "dp")


def passed_along(value, axis, by):
    size = lax.axis_size(axis)
    pairs = [(i, i + by) for i in range(size) if 0 <= i + by < size]
    return lax.ppermute(value, axis, pairs)


def from_behind(block, axis, distance):
    devices = range(lax.axis_size(axis))
    route = [((i - distance) % len(devices), i) for i in devices]
    return lax.ppermute(block, axis, route)


def pair_grads(query_rows, grad_rows, norm_rows, delta_rows, both_block):
    head_sets = query_rows.shape[0]
    length = both_block.shape[1]
    factor = HEAD_DIM ** (-0.5)
    key_part = both_block[0].reshape(length, head_sets, HEAD_DIM).transpose(1, 0, 2)
    value_part = both_block[1].reshape(length, head_sets, HEAD_DIM).transpose(1, 0, 2)
    scores = (
        jnp.einsum("kqd,kud->kqu", query_rows, key_part, preferred_element_type=jnp.float32)
        * factor
    )
    weights = jnp.exp(scores - norm_rows[:, :, None])
    weights_low = weights.astype(jnp.bfloat16)
    prob_grad = jnp.einsum(
        "kqd,kud->kqu", grad_rows, value_part, preferred_element_type=jnp.float32
    )
    score_grad = (weights * (prob_grad - delta_rows[:, :, None])).astype(jnp.bfloat16)
    query_out = (
        jnp.einsum("kqu,kud->kqd", score_grad, key_part, preferred_element_type=jnp.float32)
        * factor
    )
    key_out = (
        jnp.einsum("kqu,kqd->kud", score_grad, query_rows, preferred_element_type=jnp.float32)
        * factor
    )
    value_out = jnp.einsum(
        "kqu,kqd->kud", weights_low, grad_rows, preferred_element_type=jnp.float32
    )
    return (query_out, key_out, value_out)


def staged_reduce_scatter(partial):
    rows, width = partial.shape
    zl, xx, core, dp = (lax.axis_size(name) for name in ROW_AXES)
    block = rows // (zl * xx * core * dp)
    pieces = partial.reshape(zl, xx, core, dp, block, width).transpose(2, 1, 0, 3, 4, 5)
    here = lax.axis_index("core")
    mine = lax.dynamic_index_in_dim(pieces, here, 0, keepdims=False)
    other = lax.dynamic_index_in_dim(pieces, 1 - here, 0, keepdims=False)
    pieces = mine + lax.ppermute(other, "core", [(i, (i + 1) % core) for i in range(core)])
    pieces = lax.all_to_all(pieces, "xx", 0, 0, tiled=True).sum(0)
    pieces = pieces.reshape(zl * dp, block, width)
    return lax.all_to_all(pieces, ("zl", "dp"), 0, 0, tiled=True).sum(0)


def body(
    queries,
    key_rows,
    value_rows,
    out_grad,
    log_norm,
    row_delta,
    tok_grad,
    router_prob,
    expert_ids,
    saved_pre,
    w_down,
):
    length = queries.shape[1]
    head_sets = key_rows.shape[2] // HEAD_DIM
    group_size = HEADS // KV_HEADS
    position = lax.axis_index(CTX)

    def by_head(array):
        shaped = array[0].reshape(length, head_sets, group_size, HEAD_DIM).transpose(1, 2, 0, 3)
        return shaped.reshape(head_sets, group_size * length, HEAD_DIM)

    query_rows = by_head(queries)
    grad_rows = by_head(out_grad)
    norm_rows = log_norm[0].reshape(head_sets, group_size * length)
    delta_rows = row_delta[0].reshape(head_sets, group_size * length)
    both_local = jnp.stack([key_rows[0], value_rows[0]])
    carried_blocks = []
    current = both_local
    for repeat in range(2):
        current = passed_along(current, CTX, 1)
        carried_blocks.append(current)
    nearer = carried_blocks[0]
    farther = carried_blocks[1]
    near_mask = (position >= 1).astype(jnp.float32)
    far_mask = (position >= 2).astype(jnp.float32)
    query_near, key_near, value_near = pair_grads(
        query_rows, grad_rows, norm_rows, delta_rows, nearer
    )
    outgoing = (jnp.stack([key_near, value_near]) * near_mask).astype(jnp.bfloat16)
    arrived = from_behind(outgoing, CTX, 1)
    query_far, key_far, value_far = pair_grads(
        query_rows, grad_rows, norm_rows, delta_rows, farther
    )
    query_total = query_near * near_mask + query_far * far_mask
    query_grad = query_total.reshape(head_sets, group_size, length, HEAD_DIM).transpose(2, 0, 1, 3)
    query_grad = query_grad.reshape(1, length, head_sets * group_size * HEAD_DIM).astype(
        jnp.bfloat16
    )
    both_total = (arrived.astype(jnp.float32) + jnp.stack([key_far, value_far]) * far_mask).astype(
        jnp.bfloat16
    )
    key_grad = both_total[0].transpose(1, 0, 2).reshape(1, length, head_sets * HEAD_DIM)
    value_grad = both_total[1].transpose(1, 0, 2).reshape(1, length, head_sets * HEAD_DIM)
    expert_count = lax.axis_size("exp")
    capacity = saved_pre.shape[3] // expert_count
    model_width = tok_grad.shape[2]
    pair_count = tok_grad.shape[1] * 2
    routed = (router_prob[0][:, :, None] * tok_grad[0].astype(jnp.float32)[:, None, :]).astype(
        jnp.bfloat16
    )
    routed = routed.reshape(pair_count, model_width)
    flat_ids = expert_ids[0].reshape(pair_count)
    matches = (flat_ids[:, None] == jnp.arange(expert_count, dtype=jnp.int32)[None, :]).astype(
        jnp.int32
    )
    earlier = jnp.cumsum(matches, axis=0) - matches
    place = jnp.sum(earlier * matches, axis=1)
    slot_index = flat_ids * capacity + place
    table = (
        jnp.arange(expert_count * capacity, dtype=jnp.int32)[:, None] == slot_index[None, :]
    ).astype(jnp.bfloat16)
    outbound = jnp.dot(table, routed, preferred_element_type=jnp.float32).astype(jnp.bfloat16)
    incoming_block = lax.all_to_all(outbound, "exp", split_axis=0, concat_axis=0, tiled=True)
    saved = saved_pre[0, 0, 0].astype(jnp.float32)
    hidden_units = saved.shape[1] // 2
    gate = saved[:, :hidden_units]
    upward = saved[:, hidden_units:]
    sigma = jax.nn.sigmoid(gate)
    active = gate * sigma
    hidden_state = (active * upward).astype(jnp.bfloat16)
    hidden_gradient = jnp.einsum(
        "rd,fd->rf", incoming_block, w_down[0], preferred_element_type=jnp.float32
    )
    gate_grad = hidden_gradient * upward * sigma * (1.0 + gate * (1.0 - sigma))
    up_grad = hidden_gradient * active
    pre_grad = jnp.concatenate([gate_grad, up_grad], axis=-1).astype(jnp.bfloat16)[None, None, None]
    averaging = 1.0 / lax.axis_size(ROW_AXES)
    partial = jnp.einsum("rc,rf->cf", incoming_block, hidden_state, preferred_element_type=jnp.float32)
    summed = staged_reduce_scatter(partial)
    weight_grad = (summed * averaging)[None]
    return (query_grad, key_grad, value_grad, pre_grad, weight_grad)


def solution(mesh):
    placed = (
        P("dp", CTX, "exp"),
        P("dp", CTX, "exp"),
        P("dp", CTX, "exp"),
        P("dp", CTX, "exp"),
        P("dp", "exp", CTX),
        P("dp", "exp", CTX),
        P("dp", CTX + ("exp",), None),
        P("dp", CTX + ("exp",), None),
        P("dp", CTX + ("exp",), None),
        P("exp", CTX, "dp", None, None),
        P("exp", None, None),
    )
    ctx_size, exp_size, dp_size = mesh.devices.shape
    split = Mesh(
        mesh.devices.reshape(ctx_size // 8, 4, 2, exp_size, dp_size), ("zl", "xx", "core", "exp", "dp")
    )
    return jax.shard_map(
        body,
        mesh=split,
        in_specs=placed,
        out_specs=(
            P("dp", CTX, "exp"),
            P("dp", CTX, "exp"),
            P("dp", CTX, "exp"),
            P("exp", CTX, "dp", None, None),
            P("exp", ROW_AXES, None),
        ),
        check_vma=False,
    )
```

```python
import jax
import jax.numpy as jnp
from jax import lax
from jax.sharding import Mesh, PartitionSpec as P

HEADS = 48
KV_HEADS = 8
HEAD_DIM = 128
CTX = ("zl", "xx", "core")
ROW_AXES = ("zl", "xx", "core", "dp")


def passed_along(value, axis, by):
    size = lax.axis_size(axis)
    pairs = [(i, i + by) for i in range(size) if 0 <= i + by < size]
    return lax.ppermute(value, axis, pairs)


def from_behind(block, axis, distance):
    devices = range(lax.axis_size(axis))
    route = [((i - distance) % len(devices), i) for i in devices]
    return lax.ppermute(block, axis, route)


def pair_grads(query_rows, grad_rows, norm_rows, delta_rows, both_block):
    head_sets = query_rows.shape[0]
    length = both_block.shape[1]
    factor = HEAD_DIM ** (-0.5)
    key_part = both_block[0].reshape(length, head_sets, HEAD_DIM).transpose(1, 0, 2)
    value_part = both_block[1].reshape(length, head_sets, HEAD_DIM).transpose(1, 0, 2)
    scores = (
        jnp.einsum("kqd,kud->kqu", query_rows, key_part, preferred_element_type=jnp.float32)
        * factor
    )
    weights = jnp.exp(scores - norm_rows[:, :, None])
    weights_low = weights.astype(jnp.bfloat16)
    prob_grad = jnp.einsum(
        "kqd,kud->kqu", grad_rows, value_part, preferred_element_type=jnp.float32
    )
    score_grad = (weights * (prob_grad - delta_rows[:, :, None])).astype(jnp.bfloat16)
    query_out = (
        jnp.einsum("kqu,kud->kqd", score_grad, key_part, preferred_element_type=jnp.float32)
        * factor
    )
    key_out = (
        jnp.einsum("kqu,kqd->kud", score_grad, query_rows, preferred_element_type=jnp.float32)
        * factor
    )
    value_out = jnp.einsum(
        "kqu,kqd->kud", weights_low, grad_rows, preferred_element_type=jnp.float32
    )
    return (query_out, key_out, value_out)


def staged_reduce_scatter(partial):
    rows, width = partial.shape
    zl, xx, core, dp = (lax.axis_size(name) for name in ROW_AXES)
    block = rows // (zl * xx * core * dp)
    pieces = partial.reshape(zl, xx, core, dp, block, width).transpose(2, 1, 0, 3, 4, 5)
    here = lax.axis_index("core")
    mine = lax.dynamic_index_in_dim(pieces, here, 0, keepdims=False)
    other = lax.dynamic_index_in_dim(pieces, 1 - here, 0, keepdims=False)
    pieces = mine + lax.ppermute(other, "core", [(i, (i + 1) % core) for i in range(core)])
    pieces = lax.all_to_all(pieces.astype(jnp.bfloat16), "xx", 0, 0, tiled=True)
    pieces = pieces.astype(jnp.float32).sum(0).reshape(zl * dp, block, width)
    pieces = lax.all_to_all(pieces.astype(jnp.bfloat16), ("zl", "dp"), 0, 0, tiled=True)
    return pieces.astype(jnp.float32).sum(0)


def body(
    queries,
    key_rows,
    value_rows,
    out_grad,
    log_norm,
    row_delta,
    tok_grad,
    router_prob,
    expert_ids,
    saved_pre,
    w_down,
):
    length = queries.shape[1]
    head_sets = key_rows.shape[2] // HEAD_DIM
    group_size = HEADS // KV_HEADS
    position = lax.axis_index(CTX)

    def by_head(array):
        shaped = array[0].reshape(length, head_sets, group_size, HEAD_DIM).transpose(1, 2, 0, 3)
        return shaped.reshape(head_sets, group_size * length, HEAD_DIM)

    query_rows = by_head(queries)
    grad_rows = by_head(out_grad)
    norm_rows = log_norm[0].reshape(head_sets, group_size * length)
    delta_rows = row_delta[0].reshape(head_sets, group_size * length)
    both_local = jnp.stack([key_rows[0], value_rows[0]])
    carried_blocks = []
    current = both_local
    for repeat in range(2):
        current = passed_along(current, CTX, 1)
        carried_blocks.append(current)
    nearer = carried_blocks[0]
    farther = carried_blocks[1]
    near_mask = (position >= 1).astype(jnp.float32)
    far_mask = (position >= 2).astype(jnp.float32)
    query_near, key_near, value_near = pair_grads(
        query_rows, grad_rows, norm_rows, delta_rows, nearer
    )
    outgoing = (jnp.stack([key_near, value_near]) * near_mask).astype(jnp.bfloat16)
    arrived = from_behind(outgoing, CTX, 1)
    query_far, key_far, value_far = pair_grads(
        query_rows, grad_rows, norm_rows, delta_rows, farther
    )
    query_total = query_near * near_mask + query_far * far_mask
    query_grad = query_total.reshape(head_sets, group_size, length, HEAD_DIM).transpose(2, 0, 1, 3)
    query_grad = query_grad.reshape(1, length, head_sets * group_size * HEAD_DIM).astype(
        jnp.bfloat16
    )
    both_total = (arrived.astype(jnp.float32) + jnp.stack([key_far, value_far]) * far_mask).astype(
        jnp.bfloat16
    )
    key_grad = both_total[0].transpose(1, 0, 2).reshape(1, length, head_sets * HEAD_DIM)
    value_grad = both_total[1].transpose(1, 0, 2).reshape(1, length, head_sets * HEAD_DIM)
    expert_count = lax.axis_size("exp")
    capacity = saved_pre.shape[3] // expert_count
    model_width = tok_grad.shape[2]
    pair_count = tok_grad.shape[1] * 2
    routed = (router_prob[0][:, :, None] * tok_grad[0].astype(jnp.float32)[:, None, :]).astype(
        jnp.bfloat16
    )
    routed = routed.reshape(pair_count, model_width)
    flat_ids = expert_ids[0].reshape(pair_count)
    matches = (flat_ids[:, None] == jnp.arange(expert_count, dtype=jnp.int32)[None, :]).astype(
        jnp.int32
    )
    earlier = jnp.cumsum(matches, axis=0) - matches
    place = jnp.sum(earlier * matches, axis=1)
    slot_index = flat_ids * capacity + place
    table = (
        jnp.arange(expert_count * capacity, dtype=jnp.int32)[:, None] == slot_index[None, :]
    ).astype(jnp.bfloat16)
    outbound = jnp.dot(table, routed, preferred_element_type=jnp.float32).astype(jnp.bfloat16)
    incoming_block = lax.all_to_all(outbound, "exp", split_axis=0, concat_axis=0, tiled=True)
    saved = saved_pre[0, 0, 0].astype(jnp.float32)
    hidden_units = saved.shape[1] // 2
    gate = saved[:, :hidden_units]
    upward = saved[:, hidden_units:]
    sigma = jax.nn.sigmoid(gate)
    active = gate * sigma
    hidden_state = (active * upward).astype(jnp.bfloat16)
    hidden_gradient = jnp.einsum(
        "rd,fd->rf", incoming_block, w_down[0], preferred_element_type=jnp.float32
    )
    gate_grad = hidden_gradient * upward * sigma * (1.0 + gate * (1.0 - sigma))
    up_grad = hidden_gradient * active
    pre_grad = jnp.concatenate([gate_grad, up_grad], axis=-1).astype(jnp.bfloat16)[None, None, None]
    averaging = 1.0 / lax.axis_size(ROW_AXES)
    partial = jnp.einsum("rc,rf->cf", incoming_block, hidden_state, preferred_element_type=jnp.float32)
    summed = staged_reduce_scatter(partial)
    weight_grad = (summed * averaging)[None]
    return (query_grad, key_grad, value_grad, pre_grad, weight_grad)


def solution(mesh):
    placed = (
        P("dp", CTX, "exp"),
        P("dp", CTX, "exp"),
        P("dp", CTX, "exp"),
        P("dp", CTX, "exp"),
        P("dp", "exp", CTX),
        P("dp", "exp", CTX),
        P("dp", CTX + ("exp",), None),
        P("dp", CTX + ("exp",), None),
        P("dp", CTX + ("exp",), None),
        P("exp", CTX, "dp", None, None),
        P("exp", None, None),
    )
    ctx_size, exp_size, dp_size = mesh.devices.shape
    split = Mesh(
        mesh.devices.reshape(ctx_size // 8, 4, 2, exp_size, dp_size), ("zl", "xx", "core", "exp", "dp")
    )
    return jax.shard_map(
        body,
        mesh=split,
        in_specs=placed,
        out_specs=(
            P("dp", CTX, "exp"),
            P("dp", CTX, "exp"),
            P("dp", CTX, "exp"),
            P("exp", CTX, "dp", None, None),
            P("exp", ROW_AXES, None),
        ),
        check_vma=False,
    )
```

```python
import jax
import jax.numpy as jnp
from jax import lax
from jax.sharding import Mesh, PartitionSpec as P

HEADS = 48
KV_HEADS = 8
HEAD_DIM = 128
CTX = ("zl", "xx", "core")
ROW_AXES = ("zl", "xx", "core", "dp")


def passed_along(value, axis, by):
    size = lax.axis_size(axis)
    pairs = [(i, i + by) for i in range(size) if 0 <= i + by < size]
    return lax.ppermute(value, axis, pairs)


def from_behind(block, axis, distance):
    devices = range(lax.axis_size(axis))
    route = [((i - distance) % len(devices), i) for i in devices]
    return lax.ppermute(block, axis, route)


def pair_grads(query_rows, grad_rows, norm_rows, delta_rows, both_block):
    head_sets = query_rows.shape[0]
    length = both_block.shape[1]
    factor = HEAD_DIM ** (-0.5)
    key_part = both_block[0].reshape(length, head_sets, HEAD_DIM).transpose(1, 0, 2)
    value_part = both_block[1].reshape(length, head_sets, HEAD_DIM).transpose(1, 0, 2)
    scores = (
        jnp.einsum("kqd,kud->kqu", query_rows, key_part, preferred_element_type=jnp.float32)
        * factor
    )
    weights = jnp.exp(scores - norm_rows[:, :, None])
    weights_low = weights.astype(jnp.bfloat16)
    prob_grad = jnp.einsum(
        "kqd,kud->kqu", grad_rows, value_part, preferred_element_type=jnp.float32
    )
    score_grad = (weights * (prob_grad - delta_rows[:, :, None])).astype(jnp.bfloat16)
    query_out = (
        jnp.einsum("kqu,kud->kqd", score_grad, key_part, preferred_element_type=jnp.float32)
        * factor
    )
    key_out = (
        jnp.einsum("kqu,kqd->kud", score_grad, query_rows, preferred_element_type=jnp.float32)
        * factor
    )
    value_out = jnp.einsum(
        "kqu,kqd->kud", weights_low, grad_rows, preferred_element_type=jnp.float32
    )
    return (query_out, key_out, value_out)


def staged_reduce_scatter(partial):
    rows, width = partial.shape
    zl, xx, core, dp = (lax.axis_size(name) for name in ROW_AXES)
    block = rows // (zl * xx * core * dp)
    pieces = partial.reshape(zl, xx, core, dp, block, width).transpose(2, 1, 0, 3, 4, 5)
    here = lax.axis_index("core")
    mine = lax.dynamic_index_in_dim(pieces, here, 0, keepdims=False)
    other = lax.dynamic_index_in_dim(pieces, 1 - here, 0, keepdims=False)
    pieces = mine + lax.ppermute(other, "core", [(i, (i + 1) % core) for i in range(core)])
    pieces = lax.all_to_all(pieces.astype(jnp.bfloat16), "xx", 0, 0, tiled=True)
    pieces = pieces.astype(jnp.float32).sum(0).reshape(zl * dp, block, width)
    pieces = lax.all_to_all(pieces.astype(jnp.bfloat16), ("zl", "dp"), 0, 0, tiled=True)
    return pieces.astype(jnp.float32).sum(0)


def body(
    queries,
    key_rows,
    value_rows,
    out_grad,
    log_norm,
    row_delta,
    tok_grad,
    router_prob,
    expert_ids,
    saved_pre,
    w_down,
):
    length = queries.shape[1]
    head_sets = key_rows.shape[2] // HEAD_DIM
    group_size = HEADS // KV_HEADS
    position = lax.axis_index(CTX)

    def by_head(array):
        shaped = array[0].reshape(length, head_sets, group_size, HEAD_DIM).transpose(1, 2, 0, 3)
        return shaped.reshape(head_sets, group_size * length, HEAD_DIM)

    query_rows = by_head(queries)
    grad_rows = by_head(out_grad)
    norm_rows = log_norm[0].reshape(head_sets, group_size * length)
    delta_rows = row_delta[0].reshape(head_sets, group_size * length)
    both_local = jnp.stack([key_rows[0], value_rows[0]])
    carried_blocks = []
    current = both_local
    for repeat in range(2):
        current = passed_along(current, CTX, 1)
        carried_blocks.append(current)
    nearer = carried_blocks[0]
    farther = carried_blocks[1]
    near_mask = (position >= 1).astype(jnp.float32)
    far_mask = (position >= 2).astype(jnp.float32)
    query_near, key_near, value_near = pair_grads(
        query_rows, grad_rows, norm_rows, delta_rows, nearer
    )
    outgoing = (jnp.stack([key_near, value_near]) * near_mask).astype(jnp.bfloat16)
    arrived = from_behind(outgoing, CTX, 1)
    query_far, key_far, value_far = pair_grads(
        query_rows, grad_rows, norm_rows, delta_rows, farther
    )
    query_total = query_near * near_mask + query_far * far_mask
    query_grad = query_total.reshape(head_sets, group_size, length, HEAD_DIM).transpose(2, 0, 1, 3)
    query_grad = query_grad.reshape(1, length, head_sets * group_size * HEAD_DIM).astype(
        jnp.bfloat16
    )
    both_total = (arrived.astype(jnp.float32) + jnp.stack([key_far, value_far]) * far_mask).astype(
        jnp.bfloat16
    )
    key_grad = both_total[0].transpose(1, 0, 2).reshape(1, length, head_sets * HEAD_DIM)
    value_grad = both_total[1].transpose(1, 0, 2).reshape(1, length, head_sets * HEAD_DIM)
    expert_count = lax.axis_size("exp")
    capacity = saved_pre.shape[3] // expert_count
    model_width = tok_grad.shape[2]
    pair_count = tok_grad.shape[1] * 2
    routed = (router_prob[0][:, :, None] * tok_grad[0].astype(jnp.float32)[:, None, :]).astype(
        jnp.bfloat16
    )
    routed = routed.reshape(pair_count, model_width)
    flat_ids = expert_ids[0].reshape(pair_count)
    matches = (flat_ids[:, None] == jnp.arange(expert_count, dtype=jnp.int32)[None, :]).astype(
        jnp.int32
    )
    earlier = jnp.cumsum(matches, axis=0) - matches
    place = jnp.sum(earlier * matches, axis=1)
    slot_index = flat_ids * capacity + place
    table = (
        jnp.arange(expert_count * capacity, dtype=jnp.int32)[:, None] == slot_index[None, :]
    ).astype(jnp.bfloat16)
    outbound = jnp.dot(table, routed, preferred_element_type=jnp.float32).astype(jnp.bfloat16)
    incoming_block = lax.all_to_all(outbound, "exp", split_axis=0, concat_axis=0, tiled=True)
    incoming_block, query_grad, key_grad, value_grad = lax.optimization_barrier(
        (incoming_block, query_grad, key_grad, value_grad)
    )
    saved = saved_pre[0, 0, 0].astype(jnp.float32)
    hidden_units = saved.shape[1] // 2
    gate = saved[:, :hidden_units]
    upward = saved[:, hidden_units:]
    sigma = jax.nn.sigmoid(gate)
    active = gate * sigma
    hidden_state = (active * upward).astype(jnp.bfloat16)
    hidden_gradient = jnp.einsum(
        "rd,fd->rf", incoming_block, w_down[0], preferred_element_type=jnp.float32
    )
    gate_grad = hidden_gradient * upward * sigma * (1.0 + gate * (1.0 - sigma))
    up_grad = hidden_gradient * active
    pre_grad = jnp.concatenate([gate_grad, up_grad], axis=-1).astype(jnp.bfloat16)[None, None, None]
    averaging = 1.0 / lax.axis_size(ROW_AXES)
    partial = jnp.einsum("rc,rf->cf", incoming_block, hidden_state, preferred_element_type=jnp.float32)
    summed = staged_reduce_scatter(partial)
    weight_grad = (summed * averaging)[None]
    return (query_grad, key_grad, value_grad, pre_grad, weight_grad)


def solution(mesh):
    placed = (
        P("dp", CTX, "exp"),
        P("dp", CTX, "exp"),
        P("dp", CTX, "exp"),
        P("dp", CTX, "exp"),
        P("dp", "exp", CTX),
        P("dp", "exp", CTX),
        P("dp", CTX + ("exp",), None),
        P("dp", CTX + ("exp",), None),
        P("dp", CTX + ("exp",), None),
        P("exp", CTX, "dp", None, None),
        P("exp", None, None),
    )
    ctx_size, exp_size, dp_size = mesh.devices.shape
    split = Mesh(
        mesh.devices.reshape(ctx_size // 8, 4, 2, exp_size, dp_size), ("zl", "xx", "core", "exp", "dp")
    )
    return jax.shard_map(
        body,
        mesh=split,
        in_specs=placed,
        out_specs=(
            P("dp", CTX, "exp"),
            P("dp", CTX, "exp"),
            P("dp", CTX, "exp"),
            P("exp", CTX, "dp", None, None),
            P("exp", ROW_AXES, None),
        ),
        check_vma=False,
    )
```

```python
import jax
import jax.numpy as jnp
from jax import lax
from jax.sharding import Mesh, PartitionSpec as P

HEADS = 48
KV_HEADS = 8
HEAD_DIM = 128
CTX = ("zl", "xx", "core")
ROW_AXES = ("zl", "xx", "core", "dp")


def passed_along(value, axis, by):
    size = lax.axis_size(axis)
    pairs = [(i, i + by) for i in range(size) if 0 <= i + by < size]
    return lax.ppermute(value, axis, pairs)


def from_behind(block, axis, distance):
    devices = range(lax.axis_size(axis))
    route = [((i - distance) % len(devices), i) for i in devices]
    return lax.ppermute(block, axis, route)


def pair_grads(query_rows, grad_rows, norm_rows, delta_rows, both_block):
    head_sets = query_rows.shape[0]
    length = both_block.shape[1]
    factor = HEAD_DIM ** (-0.5)
    key_part = both_block[0].reshape(length, head_sets, HEAD_DIM).transpose(1, 0, 2)
    value_part = both_block[1].reshape(length, head_sets, HEAD_DIM).transpose(1, 0, 2)
    scores = (
        jnp.einsum("kqd,kud->kqu", query_rows, key_part, preferred_element_type=jnp.float32)
        * factor
    )
    weights = jnp.exp(scores - norm_rows[:, :, None])
    weights_low = weights.astype(jnp.bfloat16)
    prob_grad = jnp.einsum(
        "kqd,kud->kqu", grad_rows, value_part, preferred_element_type=jnp.float32
    )
    score_grad = (weights * (prob_grad - delta_rows[:, :, None])).astype(jnp.bfloat16)
    query_out = (
        jnp.einsum("kqu,kud->kqd", score_grad, key_part, preferred_element_type=jnp.float32)
        * factor
    )
    key_out = (
        jnp.einsum("kqu,kqd->kud", score_grad, query_rows, preferred_element_type=jnp.float32)
        * factor
    )
    value_out = jnp.einsum(
        "kqu,kqd->kud", weights_low, grad_rows, preferred_element_type=jnp.float32
    )
    return (query_out, key_out, value_out)


def staged_reduce_scatter(partial):
    rows, width = partial.shape
    zl, xx, core, dp = (lax.axis_size(name) for name in ROW_AXES)
    block = rows // (zl * xx * core * dp)
    pieces = partial.reshape(zl, xx, core, dp, block, width).transpose(2, 1, 0, 3, 4, 5)
    here = lax.axis_index("core")
    mine = lax.dynamic_index_in_dim(pieces, here, 0, keepdims=False)
    other = lax.dynamic_index_in_dim(pieces, 1 - here, 0, keepdims=False)
    swapped = lax.ppermute(
        other.astype(jnp.bfloat16), "core", [(i, (i + 1) % core) for i in range(core)]
    )
    pieces = mine + swapped.astype(jnp.float32)
    pieces = lax.all_to_all(pieces.astype(jnp.bfloat16), "xx", 0, 0, tiled=True)
    pieces = pieces.astype(jnp.float32).sum(0).reshape(zl * dp, block, width)
    pieces = lax.all_to_all(pieces.astype(jnp.bfloat16), ("zl", "dp"), 0, 0, tiled=True)
    return pieces.astype(jnp.float32).sum(0)


def body(
    queries,
    key_rows,
    value_rows,
    out_grad,
    log_norm,
    row_delta,
    tok_grad,
    router_prob,
    expert_ids,
    saved_pre,
    w_down,
):
    length = queries.shape[1]
    head_sets = key_rows.shape[2] // HEAD_DIM
    group_size = HEADS // KV_HEADS
    position = lax.axis_index(CTX)

    def by_head(array):
        shaped = array[0].reshape(length, head_sets, group_size, HEAD_DIM).transpose(1, 2, 0, 3)
        return shaped.reshape(head_sets, group_size * length, HEAD_DIM)

    query_rows = by_head(queries)
    grad_rows = by_head(out_grad)
    norm_rows = log_norm[0].reshape(head_sets, group_size * length)
    delta_rows = row_delta[0].reshape(head_sets, group_size * length)
    both_local = jnp.stack([key_rows[0], value_rows[0]])
    carried_blocks = []
    current = both_local
    for repeat in range(2):
        current = passed_along(current, CTX, 1)
        carried_blocks.append(current)
    nearer = carried_blocks[0]
    farther = carried_blocks[1]
    near_mask = (position >= 1).astype(jnp.float32)
    far_mask = (position >= 2).astype(jnp.float32)
    query_near, key_near, value_near = pair_grads(
        query_rows, grad_rows, norm_rows, delta_rows, nearer
    )
    outgoing = (jnp.stack([key_near, value_near]) * near_mask).astype(jnp.bfloat16)
    arrived = from_behind(outgoing, CTX, 1)
    query_far, key_far, value_far = pair_grads(
        query_rows, grad_rows, norm_rows, delta_rows, farther
    )
    query_total = query_near * near_mask + query_far * far_mask
    query_grad = query_total.reshape(head_sets, group_size, length, HEAD_DIM).transpose(2, 0, 1, 3)
    query_grad = query_grad.reshape(1, length, head_sets * group_size * HEAD_DIM).astype(
        jnp.bfloat16
    )
    both_total = (arrived.astype(jnp.float32) + jnp.stack([key_far, value_far]) * far_mask).astype(
        jnp.bfloat16
    )
    key_grad = both_total[0].transpose(1, 0, 2).reshape(1, length, head_sets * HEAD_DIM)
    value_grad = both_total[1].transpose(1, 0, 2).reshape(1, length, head_sets * HEAD_DIM)
    expert_count = lax.axis_size("exp")
    capacity = saved_pre.shape[3] // expert_count
    model_width = tok_grad.shape[2]
    pair_count = tok_grad.shape[1] * 2
    routed = (router_prob[0][:, :, None] * tok_grad[0].astype(jnp.float32)[:, None, :]).astype(
        jnp.bfloat16
    )
    routed = routed.reshape(pair_count, model_width)
    flat_ids = expert_ids[0].reshape(pair_count)
    matches = (flat_ids[:, None] == jnp.arange(expert_count, dtype=jnp.int32)[None, :]).astype(
        jnp.int32
    )
    earlier = jnp.cumsum(matches, axis=0) - matches
    place = jnp.sum(earlier * matches, axis=1)
    slot_index = flat_ids * capacity + place
    table = (
        jnp.arange(expert_count * capacity, dtype=jnp.int32)[:, None] == slot_index[None, :]
    ).astype(jnp.bfloat16)
    outbound = jnp.dot(table, routed, preferred_element_type=jnp.float32).astype(jnp.bfloat16)
    incoming_block = lax.all_to_all(outbound, "exp", split_axis=0, concat_axis=0, tiled=True)
    incoming_block, query_grad, key_grad, value_grad = lax.optimization_barrier(
        (incoming_block, query_grad, key_grad, value_grad)
    )
    saved = saved_pre[0, 0, 0].astype(jnp.float32)
    hidden_units = saved.shape[1] // 2
    gate = saved[:, :hidden_units]
    upward = saved[:, hidden_units:]
    sigma = jax.nn.sigmoid(gate)
    active = gate * sigma
    hidden_state = (active * upward).astype(jnp.bfloat16)
    hidden_gradient = jnp.einsum(
        "rd,fd->rf", incoming_block, w_down[0], preferred_element_type=jnp.float32
    )
    gate_grad = hidden_gradient * upward * sigma * (1.0 + gate * (1.0 - sigma))
    up_grad = hidden_gradient * active
    pre_grad = jnp.concatenate([gate_grad, up_grad], axis=-1).astype(jnp.bfloat16)[None, None, None]
    averaging = 1.0 / lax.axis_size(ROW_AXES)
    partial = jnp.einsum("rc,rf->cf", incoming_block, hidden_state, preferred_element_type=jnp.float32)
    summed = staged_reduce_scatter(partial)
    weight_grad = (summed * averaging)[None]
    return (query_grad, key_grad, value_grad, pre_grad, weight_grad)


def solution(mesh):
    placed = (
        P("dp", CTX, "exp"),
        P("dp", CTX, "exp"),
        P("dp", CTX, "exp"),
        P("dp", CTX, "exp"),
        P("dp", "exp", CTX),
        P("dp", "exp", CTX),
        P("dp", CTX + ("exp",), None),
        P("dp", CTX + ("exp",), None),
        P("dp", CTX + ("exp",), None),
        P("exp", CTX, "dp", None, None),
        P("exp", None, None),
    )
    ctx_size, exp_size, dp_size = mesh.devices.shape
    split = Mesh(
        mesh.devices.reshape(ctx_size // 8, 4, 2, exp_size, dp_size), ("zl", "xx", "core", "exp", "dp")
    )
    return jax.shard_map(
        body,
        mesh=split,
        in_specs=placed,
        out_specs=(
            P("dp", CTX, "exp"),
            P("dp", CTX, "exp"),
            P("dp", CTX, "exp"),
            P("exp", CTX, "dp", None, None),
            P("exp", ROW_AXES, None),
        ),
        check_vma=False,
    )
```

```python
import jax
import jax.numpy as jnp
from jax import lax
from jax.sharding import Mesh, PartitionSpec as P

HEADS = 48
KV_HEADS = 8
HEAD_DIM = 128
CTX = ("zl", "xx", "core")
ROW_AXES = ("zl", "xx", "core", "dp")


def passed_along(value, axis, by):
    size = lax.axis_size(axis)
    pairs = [(i, i + by) for i in range(size) if 0 <= i + by < size]
    return lax.ppermute(value, axis, pairs)


def from_behind(block, axis, distance):
    devices = range(lax.axis_size(axis))
    route = [((i - distance) % len(devices), i) for i in devices]
    return lax.ppermute(block, axis, route)


def pair_grads(query_rows, grad_rows, norm_rows, delta_rows, both_block):
    head_sets = query_rows.shape[0]
    length = both_block.shape[1]
    factor = HEAD_DIM ** (-0.5)
    key_part = both_block[0].reshape(length, head_sets, HEAD_DIM).transpose(1, 0, 2)
    value_part = both_block[1].reshape(length, head_sets, HEAD_DIM).transpose(1, 0, 2)
    scores = (
        jnp.einsum("kqd,kud->kqu", query_rows, key_part, preferred_element_type=jnp.float32)
        * factor
    )
    weights = jnp.exp(scores - norm_rows[:, :, None])
    weights_low = weights.astype(jnp.bfloat16)
    prob_grad = jnp.einsum(
        "kqd,kud->kqu", grad_rows, value_part, preferred_element_type=jnp.float32
    )
    score_grad = (weights * (prob_grad - delta_rows[:, :, None])).astype(jnp.bfloat16)
    query_out = (
        jnp.einsum("kqu,kud->kqd", score_grad, key_part, preferred_element_type=jnp.float32)
        * factor
    )
    key_out = (
        jnp.einsum("kqu,kqd->kud", score_grad, query_rows, preferred_element_type=jnp.float32)
        * factor
    )
    value_out = jnp.einsum(
        "kqu,kqd->kud", weights_low, grad_rows, preferred_element_type=jnp.float32
    )
    return (query_out, key_out, value_out)


def staged_reduce_scatter(partial):
    rows, width = partial.shape
    zl, xx, core, dp = (lax.axis_size(name) for name in ROW_AXES)
    block = rows // (zl * xx * core * dp)
    pieces = partial.reshape(zl, xx, core, dp, block, width).transpose(2, 1, 0, 3, 4, 5)
    here = lax.axis_index("core")
    mine = lax.dynamic_index_in_dim(pieces, here, 0, keepdims=False)
    other = lax.dynamic_index_in_dim(pieces, 1 - here, 0, keepdims=False)
    pieces = mine + lax.ppermute(other, "core", [(i, (i + 1) % core) for i in range(core)])
    pieces = lax.all_to_all(pieces.astype(jnp.bfloat16), "xx", 0, 0, tiled=True)
    pieces = pieces.astype(jnp.float32).sum(0).reshape(zl * dp, block, width)
    pieces = lax.all_to_all(pieces.astype(jnp.bfloat16), ("zl", "dp"), 0, 0, tiled=True)
    return pieces.astype(jnp.float32).sum(0)


def body(
    queries,
    key_rows,
    value_rows,
    out_grad,
    log_norm,
    row_delta,
    tok_grad,
    router_prob,
    expert_ids,
    saved_pre,
    w_down,
):
    length = queries.shape[1]
    head_sets = key_rows.shape[2] // HEAD_DIM
    group_size = HEADS // KV_HEADS
    position = lax.axis_index(CTX)

    def by_head(array):
        shaped = array[0].reshape(length, head_sets, group_size, HEAD_DIM).transpose(1, 2, 0, 3)
        return shaped.reshape(head_sets, group_size * length, HEAD_DIM)

    query_rows = by_head(queries)
    grad_rows = by_head(out_grad)
    norm_rows = log_norm[0].reshape(head_sets, group_size * length)
    delta_rows = row_delta[0].reshape(head_sets, group_size * length)
    both_local = jnp.stack([key_rows[0], value_rows[0]])
    carried_blocks = []
    current = both_local
    for repeat in range(2):
        current = passed_along(current, CTX, 1)
        carried_blocks.append(current)
    nearer = carried_blocks[0]
    farther = carried_blocks[1]
    near_mask = (position >= 1).astype(jnp.float32)
    far_mask = (position >= 2).astype(jnp.float32)
    query_near, key_near, value_near = pair_grads(
        query_rows, grad_rows, norm_rows, delta_rows, nearer
    )
    outgoing = (jnp.stack([key_near, value_near]) * near_mask).astype(jnp.bfloat16)
    arrived = from_behind(outgoing, CTX, 1)
    query_far, key_far, value_far = pair_grads(
        query_rows, grad_rows, norm_rows, delta_rows, farther
    )
    query_total = query_near * near_mask + query_far * far_mask
    query_grad = query_total.reshape(head_sets, group_size, length, HEAD_DIM).transpose(2, 0, 1, 3)
    query_grad = query_grad.reshape(1, length, head_sets * group_size * HEAD_DIM).astype(
        jnp.bfloat16
    )
    both_total = (arrived.astype(jnp.float32) + jnp.stack([key_far, value_far]) * far_mask).astype(
        jnp.bfloat16
    )
    key_grad = both_total[0].transpose(1, 0, 2).reshape(1, length, head_sets * HEAD_DIM)
    value_grad = both_total[1].transpose(1, 0, 2).reshape(1, length, head_sets * HEAD_DIM)
    expert_count = lax.axis_size("exp")
    capacity = saved_pre.shape[3] // expert_count
    model_width = tok_grad.shape[2]
    pair_count = tok_grad.shape[1] * 2
    flat_ids = expert_ids[0].reshape(pair_count)
    matches = (flat_ids[:, None] == jnp.arange(expert_count, dtype=jnp.int32)[None, :]).astype(
        jnp.int32
    )
    earlier = jnp.cumsum(matches, axis=0) - matches
    place = jnp.sum(earlier * matches, axis=1)
    slot_index = flat_ids * capacity + place
    hit = jnp.arange(expert_count * capacity, dtype=jnp.int32)[:, None] == slot_index[None, :]
    token_table = hit.reshape(expert_count * capacity, pair_count // 2, 2).any(axis=2)
    slot_prob = jnp.sum(jnp.where(hit, router_prob[0].reshape(pair_count)[None, :], 0.0), axis=1)
    picked = jnp.dot(
        token_table.astype(jnp.bfloat16), tok_grad[0], preferred_element_type=jnp.float32
    )
    outbound = (slot_prob[:, None] * picked).astype(jnp.bfloat16)
    incoming_block = lax.all_to_all(outbound, "exp", split_axis=0, concat_axis=0, tiled=True)
    incoming_block, query_grad, key_grad, value_grad = lax.optimization_barrier(
        (incoming_block, query_grad, key_grad, value_grad)
    )
    saved = saved_pre[0, 0, 0].astype(jnp.float32)
    hidden_units = saved.shape[1] // 2
    gate = saved[:, :hidden_units]
    upward = saved[:, hidden_units:]
    sigma = jax.nn.sigmoid(gate)
    active = gate * sigma
    hidden_state = (active * upward).astype(jnp.bfloat16)
    hidden_gradient = jnp.einsum(
        "rd,fd->rf", incoming_block, w_down[0], preferred_element_type=jnp.float32
    )
    gate_grad = hidden_gradient * upward * sigma * (1.0 + gate * (1.0 - sigma))
    up_grad = hidden_gradient * active
    pre_grad = jnp.concatenate([gate_grad, up_grad], axis=-1).astype(jnp.bfloat16)[None, None, None]
    averaging = 1.0 / lax.axis_size(ROW_AXES)
    partial = jnp.einsum("rc,rf->cf", incoming_block, hidden_state, preferred_element_type=jnp.float32)
    summed = staged_reduce_scatter(partial)
    weight_grad = (summed * averaging)[None]
    return (query_grad, key_grad, value_grad, pre_grad, weight_grad)


def solution(mesh):
    placed = (
        P("dp", CTX, "exp"),
        P("dp", CTX, "exp"),
        P("dp", CTX, "exp"),
        P("dp", CTX, "exp"),
        P("dp", "exp", CTX),
        P("dp", "exp", CTX),
        P("dp", CTX + ("exp",), None),
        P("dp", CTX + ("exp",), None),
        P("dp", CTX + ("exp",), None),
        P("exp", CTX, "dp", None, None),
        P("exp", None, None),
    )
    ctx_size, exp_size, dp_size = mesh.devices.shape
    split = Mesh(
        mesh.devices.reshape(ctx_size // 8, 4, 2, exp_size, dp_size), ("zl", "xx", "core", "exp", "dp")
    )
    return jax.shard_map(
        body,
        mesh=split,
        in_specs=placed,
        out_specs=(
            P("dp", CTX, "exp"),
            P("dp", CTX, "exp"),
            P("dp", CTX, "exp"),
            P("exp", CTX, "dp", None, None),
            P("exp", ROW_AXES, None),
        ),
        check_vma=False,
    )
```

```python
import jax
import jax.numpy as jnp
from jax import lax
from jax.sharding import Mesh, PartitionSpec as P

HEADS = 48
KV_HEADS = 8
HEAD_DIM = 128
CTX = ("zl", "xx", "core")
ROW_AXES = ("zl", "xx", "core", "dp")


def passed_along(value, axis, by):
    size = lax.axis_size(axis)
    pairs = [(i, i + by) for i in range(size) if 0 <= i + by < size]
    return lax.ppermute(value, axis, pairs)


def from_behind(block, axis, distance):
    devices = range(lax.axis_size(axis))
    route = [((i - distance) % len(devices), i) for i in devices]
    return lax.ppermute(block, axis, route)


def pair_grads(query_rows, grad_rows, norm_rows, delta_rows, both_block):
    head_sets = query_rows.shape[0]
    length = both_block.shape[1]
    factor = HEAD_DIM ** (-0.5)
    key_part = both_block[0].reshape(length, head_sets, HEAD_DIM).transpose(1, 0, 2)
    value_part = both_block[1].reshape(length, head_sets, HEAD_DIM).transpose(1, 0, 2)
    scores = (
        jnp.einsum("kqd,kud->kqu", query_rows, key_part, preferred_element_type=jnp.float32)
        * factor
    )
    weights = jnp.exp(scores - norm_rows[:, :, None])
    weights_low = weights.astype(jnp.bfloat16)
    prob_grad = jnp.einsum(
        "kqd,kud->kqu", grad_rows, value_part, preferred_element_type=jnp.float32
    )
    score_grad = (weights * (prob_grad - delta_rows[:, :, None])).astype(jnp.bfloat16)
    query_out = (
        jnp.einsum("kqu,kud->kqd", score_grad, key_part, preferred_element_type=jnp.float32)
        * factor
    )
    key_out = (
        jnp.einsum("kqu,kqd->kud", score_grad, query_rows, preferred_element_type=jnp.float32)
        * factor
    )
    value_out = jnp.einsum(
        "kqu,kqd->kud", weights_low, grad_rows, preferred_element_type=jnp.float32
    )
    return (query_out, key_out, value_out)


def staged_reduce_scatter(partial):
    rows, width = partial.shape
    zl, xx, core, dp = (lax.axis_size(name) for name in ROW_AXES)
    block = rows // (zl * xx * core * dp)
    pieces = partial.reshape(zl, xx, core, dp, block, width).transpose(2, 1, 0, 3, 4, 5)
    here = lax.axis_index("core")
    mine = lax.dynamic_index_in_dim(pieces, here, 0, keepdims=False)
    other = lax.dynamic_index_in_dim(pieces, 1 - here, 0, keepdims=False)
    pieces = mine + lax.ppermute(other, "core", [(i, (i + 1) % core) for i in range(core)])
    pieces = lax.all_to_all(pieces.astype(jnp.bfloat16), "xx", 0, 0, tiled=True)
    pieces = pieces.astype(jnp.float32).sum(0).reshape(zl * dp, block, width)
    pieces = lax.all_to_all(pieces.astype(jnp.bfloat16), ("zl", "dp"), 0, 0, tiled=True)
    return pieces.astype(jnp.float32).sum(0)


def body(
    queries,
    key_rows,
    value_rows,
    out_grad,
    log_norm,
    row_delta,
    tok_grad,
    router_prob,
    expert_ids,
    saved_pre,
    w_down,
):
    expert_count = lax.axis_size("exp")
    capacity = saved_pre.shape[3] // expert_count
    model_width = tok_grad.shape[2]
    pair_count = tok_grad.shape[1] * 2
    flat_ids = expert_ids[0].reshape(pair_count)
    matches = (flat_ids[:, None] == jnp.arange(expert_count, dtype=jnp.int32)[None, :]).astype(
        jnp.int32
    )
    earlier = jnp.cumsum(matches, axis=0) - matches
    place = jnp.sum(earlier * matches, axis=1)
    slot_index = flat_ids * capacity + place
    hit = jnp.arange(expert_count * capacity, dtype=jnp.int32)[:, None] == slot_index[None, :]
    token_table = hit.reshape(expert_count * capacity, pair_count // 2, 2).any(axis=2)
    slot_prob = jnp.sum(jnp.where(hit, router_prob[0].reshape(pair_count)[None, :], 0.0), axis=1)
    picked = jnp.dot(
        token_table.astype(jnp.bfloat16), tok_grad[0], preferred_element_type=jnp.float32
    )
    outbound = (slot_prob[:, None] * picked).astype(jnp.bfloat16)
    outbound, queries, key_rows, value_rows, out_grad, log_norm, row_delta = lax.optimization_barrier(
        (outbound, queries, key_rows, value_rows, out_grad, log_norm, row_delta)
    )
    length = queries.shape[1]
    head_sets = key_rows.shape[2] // HEAD_DIM
    group_size = HEADS // KV_HEADS
    position = lax.axis_index(CTX)

    def by_head(array):
        shaped = array[0].reshape(length, head_sets, group_size, HEAD_DIM).transpose(1, 2, 0, 3)
        return shaped.reshape(head_sets, group_size * length, HEAD_DIM)

    query_rows = by_head(queries)
    grad_rows = by_head(out_grad)
    norm_rows = log_norm[0].reshape(head_sets, group_size * length)
    delta_rows = row_delta[0].reshape(head_sets, group_size * length)
    both_local = jnp.stack([key_rows[0], value_rows[0]])
    carried_blocks = []
    current = both_local
    for repeat in range(2):
        current = passed_along(current, CTX, 1)
        carried_blocks.append(current)
    nearer = carried_blocks[0]
    farther = carried_blocks[1]
    near_mask = (position >= 1).astype(jnp.float32)
    far_mask = (position >= 2).astype(jnp.float32)
    query_near, key_near, value_near = pair_grads(
        query_rows, grad_rows, norm_rows, delta_rows, nearer
    )
    outgoing = (jnp.stack([key_near, value_near]) * near_mask).astype(jnp.bfloat16)
    arrived = from_behind(outgoing, CTX, 1)
    query_far, key_far, value_far = pair_grads(
        query_rows, grad_rows, norm_rows, delta_rows, farther
    )
    query_total = query_near * near_mask + query_far * far_mask
    query_grad = query_total.reshape(head_sets, group_size, length, HEAD_DIM).transpose(2, 0, 1, 3)
    query_grad = query_grad.reshape(1, length, head_sets * group_size * HEAD_DIM).astype(
        jnp.bfloat16
    )
    both_total = (arrived.astype(jnp.float32) + jnp.stack([key_far, value_far]) * far_mask).astype(
        jnp.bfloat16
    )
    key_grad = both_total[0].transpose(1, 0, 2).reshape(1, length, head_sets * HEAD_DIM)
    value_grad = both_total[1].transpose(1, 0, 2).reshape(1, length, head_sets * HEAD_DIM)
    incoming_block = lax.all_to_all(outbound, "exp", split_axis=0, concat_axis=0, tiled=True)
    incoming_block, query_grad, key_grad, value_grad = lax.optimization_barrier(
        (incoming_block, query_grad, key_grad, value_grad)
    )
    saved = saved_pre[0, 0, 0].astype(jnp.float32)
    hidden_units = saved.shape[1] // 2
    gate = saved[:, :hidden_units]
    upward = saved[:, hidden_units:]
    sigma = jax.nn.sigmoid(gate)
    active = gate * sigma
    hidden_state = (active * upward).astype(jnp.bfloat16)
    hidden_gradient = jnp.einsum(
        "rd,fd->rf", incoming_block, w_down[0], preferred_element_type=jnp.float32
    )
    gate_grad = hidden_gradient * upward * sigma * (1.0 + gate * (1.0 - sigma))
    up_grad = hidden_gradient * active
    pre_grad = jnp.concatenate([gate_grad, up_grad], axis=-1).astype(jnp.bfloat16)[None, None, None]
    averaging = 1.0 / lax.axis_size(ROW_AXES)
    partial = jnp.einsum("rc,rf->cf", incoming_block, hidden_state, preferred_element_type=jnp.float32)
    summed = staged_reduce_scatter(partial)
    weight_grad = (summed * averaging)[None]
    return (query_grad, key_grad, value_grad, pre_grad, weight_grad)


def solution(mesh):
    placed = (
        P("dp", CTX, "exp"),
        P("dp", CTX, "exp"),
        P("dp", CTX, "exp"),
        P("dp", CTX, "exp"),
        P("dp", "exp", CTX),
        P("dp", "exp", CTX),
        P("dp", CTX + ("exp",), None),
        P("dp", CTX + ("exp",), None),
        P("dp", CTX + ("exp",), None),
        P("exp", CTX, "dp", None, None),
        P("exp", None, None),
    )
    ctx_size, exp_size, dp_size = mesh.devices.shape
    split = Mesh(
        mesh.devices.reshape(ctx_size // 8, 4, 2, exp_size, dp_size), ("zl", "xx", "core", "exp", "dp")
    )
    return jax.shard_map(
        body,
        mesh=split,
        in_specs=placed,
        out_specs=(
            P("dp", CTX, "exp"),
            P("dp", CTX, "exp"),
            P("dp", CTX, "exp"),
            P("exp", CTX, "dp", None, None),
            P("exp", ROW_AXES, None),
        ),
        check_vma=False,
    )
```
